256 devices in a mesh: dp: 32 (over y, z), expert: 8 (over x, core).
Axes of the slice: x: 4, y: 4, z: 8, core: 2. Of those that a mesh axis runs over, the one named last changes fastest.
Arguments:
- master: float32 [8, 4096, 1536], P('expert', 'dp'), may hold values from -0.109375 to 0.109375
- moment_one: float32 [8, 4096, 1536], P('expert', 'dp'), may hold values from -1.5 to 1.5
- moment_two: float32 [8, 4096, 1536], P('expert', 'dp'), may hold values from 0.0001 to 0.003
- saved_rows: bfloat16 [8, 12288, 1536], P('expert', 'dp'), may hold values from -6 to 6
- saved_grads: bfloat16 [8, 12288, 4096], P('expert', 'dp'), may hold values from -0.109375 to 0.109375
- slot_rows: bfloat16 [32768, 2, 1536], P(('dp', 'expert')), may hold values from -6 to 6
- routes: int32 [32768, 2], P(('dp', 'expert')), may hold values from 0 to 7, all different within a row; in each aligned block of 128 rows (0 to 127, 128 to 255, ...) at most 40 rows name the same one
- gates: float32 [32768, 2], P(('dp', 'expert')), may hold values from 0.1 to 1
Outputs:
- master_new: float32 [8, 4096, 1536], P('expert', 'dp')
- moment_one_new: float32 [8, 4096, 1536], P('expert', 'dp')
- moment_two_new: float32 [8, 4096, 1536], P('expert', 'dp')
- mixed: bfloat16 [32768, 4096], P(('dp', 'expert'))
The draws below stay inside these ranges and needn't reach their ends.
Inputs may be any that keep to these rules, and one draw needn't show every extreme that they name: `routes`: each token names 2 different experts. Among the 128 tokens of one device (aligned blocks of rows in device order, dp slowest) at most 40 name the same expert, and in some device's block exactly 40 do.
All inputs are finite; a program needn't handle non-finite values.
Results may differ from the reference program's by a relative error of at most 0.034.
Values may be sent and summed in bfloat16 or wider, within the bound.
No kernel may reach another device: no remote copies, remote signals or barrier semaphores. Data moves between devices by JAX's collectives and lax.ppermute only.
A program may use at most 128 MiB of HBM per device.

```python
import math
import jax
import jax.numpy as jnp
import numpy as np
from jax import lax

D = 4096
FF = 1536
TOPK = 2
TOK_DEV = 128
SAVED = 384
EXPERTS = 8
CAP = 40
TOKENS = 32768
N_DP = 32


def strengthened(entries, rng, source, target, parts, factor):
    owner, partner = [(jnp.arange(entries.shape[dim]) // (entries.shape[dim] // parts)).reshape([-1 if axis == dim else 1 for axis in range(entries.ndim)]) for dim in (source, target)]
    chosen = jax.random.permutation(rng, parts)[partner]
    strong = (owner == chosen) | (owner == (partner + parts // 2) % parts)
    return jnp.where(strong, factor * entries, entries)


def block_scale(own_key, extent, pieces, least, largest):
    factor_of, own = 1.0, jax.random.fold_in(own_key, 6)
    for position, shards_of in pieces:
        steps = jnp.exp(jax.random.uniform(jax.random.fold_in(own, position), (shards_of,), jnp.float32, least / len(pieces), largest / len(pieces)))
        factor_of = factor_of * jnp.repeat(steps, extent[position] // shards_of).reshape([-1 if axis == position else 1 for axis in range(len(extent))])
    return factor_of


def deal_out(rng, own, number, rows, amount, top, most, lean):
    sequence = jax.random.permutation(rng, amount)
    heavy_load, usual = load_shares(amount, rows * top, most, lean, True), load_shares(amount, rows * top, most, lean, False)
    places = jnp.arange(amount)

    def named(lengths, offset_by):
        used = int((lengths > 0).sum())
        fixed = max(1, used // 4)
        moved = fixed + (places - fixed + offset_by * (used - fixed)) % max(1, amount - fixed)
        return jnp.zeros((amount,), jnp.int32).at[sequence[jnp.where(places < fixed, places, moved)]].set(jnp.asarray(lengths, jnp.int32))

    lengths = jnp.where(number % 4 == 0, named(heavy_load, number // 4), named(usual, number - number // 4 - 1))
    mixed = jax.random.permutation(jax.random.fold_in(own, 3), amount)
    source_of, taker = mixed[0:amount // 2 * 2:2], mixed[1:amount // 2 * 2:2]
    slack = jnp.minimum(lengths[source_of] - 1, most - lengths[taker]) // 2
    slack = jnp.where((source_of == sequence[0]) | (taker == sequence[0]) | (lengths[taker] == 0), 0, jnp.maximum(slack, 0))
    moved = jax.random.randint(jax.random.fold_in(own, 4), (amount // 2,), 0, 1 << 20) % (slack + 1)
    lengths = lengths.at[source_of].add(-moved).at[taker].add(moved)
    members = jnp.searchsorted(jnp.cumsum(lengths), jnp.arange(rows * top), side="right").astype(jnp.int32)
    listing = members.reshape(top, rows).T
    listing = listing[jax.random.permutation(jax.random.fold_in(own, 1), rows)]
    offset_by = jax.random.randint(jax.random.fold_in(own, 2), (rows, 1), 0, top)
    return jnp.take_along_axis(listing, (jnp.arange(top)[None, :] + offset_by) % top, axis=1)


def load_shares(number_of, total, most, lean, full):
    weights = [(1 << 20) // math.isqrt(rank ** lean) + 1 for rank in range(1, number_of + 1)]
    largest = most if full else min(most, max(-(-total // number_of), total * weights[0] // sum(weights)))
    least = 1 if total - largest >= number_of - 1 else 0
    holding, surplus = [largest] + [least] * (number_of - 1), total - largest - least * (number_of - 1)
    while surplus > 0:
        candidates = [i for i in range(1, number_of) if holding[i] < largest] or [i for i in range(1, number_of) if holding[i] < most]
        pool, budget = sum([weights[i] for i in candidates]), surplus
        for i in candidates:
            extra = min(most - holding[i], max(1, budget * weights[i] // pool), surplus)
            holding[i] = holding[i] + extra
            surplus = surplus - extra
    return np.array(holding)


def gaussian(key, dims, deviation, reach, split=(), kind=jnp.bfloat16):
    drawn = deviation * jax.random.normal(key, dims, jnp.float32)
    if split:
        drawn = drawn * block_scale(key, dims, split, -0.22, 0.18)
    return jnp.clip(drawn, -reach, reach).astype(kind)


def noise_with(rng, dims, scale, limit, pieces, heavy, kind=jnp.bfloat16):
    entries = scale * jax.random.normal(rng, dims, jnp.float32)
    if pieces:
        entries = entries * block_scale(rng, dims, pieces, -0.22, 0.18)
    return jnp.clip(strengthened(entries, jax.random.fold_in(rng, 3), *heavy), -limit, limit).astype(kind)


def setup_inputs(seed: int = 0) -> dict:
    key_list = jax.random.split(jax.random.key(seed), 9)
    master = gaussian(key_list[0], (EXPERTS, D, FF), (2 * FF) ** -0.5, 0.109375, ((0, 8), (1, 32)), jnp.float32)
    moment_one = gaussian(key_list[1], (EXPERTS, D, FF), 0.1, 1.5, ((0, 8), (1, 32)), jnp.float32)
    moment_two = jnp.clip(jnp.exp(math.log(0.003) - 3.4011974 * jax.random.uniform(key_list[2], (EXPERTS, D, FF), jnp.float32) ** block_scale(key_list[2], (EXPERTS, D, FF), ((0, 8), (1, 32)), -0.2, 0.2)), 0.0001, 0.003)
    saved_rows = gaussian(key_list[3], (EXPERTS, SAVED * N_DP, FF), 1.0, 6.0, ((0, 8), (1, 32)))
    saved_grads = noise_with(key_list[4], (EXPERTS, SAVED * N_DP, D), (SAVED * N_DP) ** -0.5, 0.109375, ((0, 8), (1, 32)), (1, 2, 32, 2.75))
    slot_rows = gaussian(key_list[5], (TOKENS, TOPK, FF), 1.0, 6.0, ((0, 256),))
    routes_keys = jax.random.split(jax.random.fold_in(key_list[6], 1), TOKENS // TOK_DEV)
    routes_turns = jax.random.permutation(jax.random.fold_in(key_list[6], 3), TOKENS // TOK_DEV)
    routes = jax.vmap(lambda own, number: deal_out(jax.random.fold_in(key_list[6], 2), own, number, TOK_DEV, EXPERTS, TOPK, CAP, 2))(routes_keys, routes_turns).reshape((TOKENS, TOPK))
    gates = jnp.clip(0.1 + 0.9 * jax.random.uniform(key_list[7], (TOKENS, TOPK), jnp.float32) ** block_scale(key_list[7], (TOKENS, TOPK), ((0, 256),), -0.2, 0.2), 0.1, 1.0)
    return dict(master=master, moment_one=moment_one, moment_two=moment_two, saved_rows=saved_rows, saved_grads=saved_grads, slot_rows=slot_rows, routes=routes, gates=gates)


beta_one = 0.9
beta_two = 0.999
learn_rate = 0.002
tiny_eps = 1e-08
steps_done = 100.0

def adam_update(master, moment_one, moment_two, grad):
    m_new = beta_one * moment_one + (1.0 - beta_one) * grad
    v_new = beta_two * moment_two + (1.0 - beta_two) * grad * grad
    fix_one = 1.0 - beta_one ** steps_done
    fix_two = 1.0 - beta_two ** steps_done
    step_size = m_new / fix_one / (jnp.sqrt(v_new / fix_two) + tiny_eps)
    return (master - learn_rate * step_size, m_new, v_new)

def reference(master, moment_one, moment_two, saved_rows, saved_grads, slot_rows, routes, gates):

    def expert_grad(pair):
        rows = pair[0].reshape(N_DP, SAVED, FF)
        grads = pair[1].reshape(N_DP, SAVED, D)

        def add_part(total, piece):
            part = lax.dot_general(piece[1], piece[0], (((0,), (0,)), ((), ())), preferred_element_type=jnp.float32)
            part = lax.optimization_barrier(part.astype(jnp.bfloat16))
            return (total + part.astype(jnp.float32), None)
        total, _ = lax.scan(add_part, jnp.zeros((D, FF), jnp.float32), (rows, grads))
        return total
    grad = lax.map(expert_grad, (saved_rows, saved_grads))
    master_new, m_new, v_new = adam_update(master, moment_one, moment_two, grad)
    weights = master_new.astype(jnp.bfloat16)
    blocks = TOKENS // TOK_DEV
    width = TOK_DEV * TOPK
    flat = routes.reshape(blocks, width).astype(jnp.int32)
    onehot = (flat[:, :, None] == jnp.arange(EXPERTS, dtype=jnp.int32)[None, None, :]).astype(jnp.int32)
    place = lax.optimization_barrier(jnp.sum((jnp.cumsum(onehot, axis=1) - onehot) * onehot, axis=2)).astype(jnp.int32)
    rows_all = slot_rows.reshape(blocks, width, FF)
    block_ids = jnp.broadcast_to(jnp.arange(blocks, dtype=jnp.int32)[:, None], (blocks, width))

    def expert_out(pair):
        expert_id, weight = pair
        index = jnp.where(flat == expert_id, place, CAP).astype(jnp.int32)
        table = jnp.zeros((blocks, CAP + 1, FF), jnp.bfloat16).at[block_ids, index].set(rows_all)
        outs = lax.dot_general(table[:, :CAP].reshape(blocks * CAP, FF), weight, (((1,), (1,)), ((), ())), preferred_element_type=jnp.float32)
        return outs.astype(jnp.bfloat16).reshape(blocks, CAP, D)
    served = lax.map(expert_out, (jnp.arange(EXPERTS, dtype=jnp.int32), weights))

    def block_mix(item):
        block_id, experts_here, places_here, gate_here = item
        picked = served[experts_here, block_id, places_here].astype(jnp.float32)
        picked = picked.reshape(TOK_DEV, TOPK, D) * gate_here.reshape(TOK_DEV, TOPK)[:, :, None]
        return lax.optimization_barrier(jnp.sum(picked, axis=1)).astype(jnp.bfloat16)
    mixed = lax.map(block_mix, (jnp.arange(blocks, dtype=jnp.int32), flat, place, gates.reshape(blocks, width)))
    return (master_new, m_new, v_new, mixed.reshape(TOKENS, D))
```

```python
import jax
import jax.numpy as jnp
import numpy as np
from jax import lax
from jax.sharding import Mesh
from jax.sharding import PartitionSpec as P

beta_one = 0.9
beta_two = 0.999
learn_rate = 0.002
tiny_eps = 1e-08
steps_done = 100.0


def adam_update(master, moment_one, moment_two, grad):
    m_new = beta_one * moment_one + (1.0 - beta_one) * grad
    v_new = beta_two * moment_two + (1.0 - beta_two) * grad * grad
    fix_one = 1.0 - beta_one**steps_done
    fix_two = 1.0 - beta_two**steps_done
    step_size = m_new / fix_one / (jnp.sqrt(v_new / fix_two) + tiny_eps)
    return (master - learn_rate * step_size, m_new, v_new)


def slot_places(routes, experts):
    flat = routes.reshape(-1)
    onehot = (flat[:, None] == jnp.arange(experts, dtype=jnp.int32)[None, :]).astype(jnp.int32)
    place = jnp.sum((jnp.cumsum(onehot, axis=0) - onehot) * onehot, axis=1)
    return (flat, place)


def body(master, moment_one, moment_two, saved_rows, saved_grads, slot_rows, routes, gates):
    n_hi = lax.axis_size("dy")
    n_lo = lax.axis_size("dz")
    experts = lax.axis_size("expert")

    rows_here = saved_rows[0]
    grads_here = saved_grads[0]
    saved, d_model = grads_here.shape
    group_width = d_model // n_hi
    rows_group = lax.all_gather(rows_here, "dy", axis=0, tiled=True)
    grads_group = lax.all_to_all(
        grads_here.reshape(saved, n_hi, group_width).transpose(1, 0, 2),
        "dy",
        split_axis=0,
        concat_axis=0,
        tiled=True,
    ).reshape(n_hi * saved, group_width)
    partial = lax.dot_general(
        grads_group, rows_group, (((0,), (0,)), ((), ())), preferred_element_type=jnp.float32
    ).astype(jnp.bfloat16)
    grad = lax.psum_scatter(partial, "dz", scatter_dimension=0, tiled=True).astype(jnp.float32)
    master_new, m_new, v_new = adam_update(master[0], moment_one[0], moment_two[0], grad)
    weights_shard = master_new.astype(jnp.bfloat16)

    tok_count, top_count, width = slot_rows.shape
    capacity = tok_count * top_count * 5 // (4 * experts)
    flat, place = slot_places(routes, experts)
    slot_id = flat * capacity + place
    table = jnp.arange(experts * capacity, dtype=jnp.int32)
    select = (table[:, None] == slot_id[None, :]).astype(jnp.bfloat16)
    outgoing = lax.dot_general(
        select, slot_rows.reshape(-1, width), (((1,), (0,)), ((), ())),
        preferred_element_type=jnp.float32,
    ).astype(jnp.bfloat16).reshape(experts, capacity, width)
    received = lax.all_to_all(outgoing, "expert", split_axis=0, concat_axis=0, tiled=True)
    slots_group = lax.all_gather(received, "dy", axis=0, tiled=True).reshape(-1, width)

    weights_group = lax.all_gather(weights_shard, "dz", axis=0, tiled=True)
    product = lax.dot_general(
        slots_group, weights_group, (((1,), (1,)), ((), ())), preferred_element_type=jnp.float32
    ).astype(jnp.bfloat16)
    returned = lax.all_to_all(
        product, ("dy", "expert"), split_axis=0, concat_axis=0, tiled=True
    ).reshape(n_hi, experts * capacity, group_width)

    slot_pairs = slot_id.reshape(tok_count, top_count)
    combine = jnp.sum(
        (slot_pairs[:, :, None] == table[None, None, :]).astype(jnp.float32) * gates[:, :, None],
        axis=1,
    )
    mixed = jnp.einsum(
        "ts,hsf->thf",
        combine,
        returned.astype(jnp.float32),
        precision=lax.Precision.HIGHEST,
        preferred_element_type=jnp.float32,
    )
    mixed = mixed.reshape(tok_count, n_hi * group_width).astype(jnp.bfloat16)
    return (master_new[None], m_new[None], v_new[None], mixed)


def split_mesh(mesh):
    devices = mesh.devices
    dp_size, ex_size = devices.shape
    column = devices[:, 0]
    try:
        n_hi = len({d.coords[1] for d in column})
    except Exception:
        n_hi = 1
    if n_hi < 1 or dp_size % n_hi:
        n_hi = 1
    return Mesh(devices.reshape(n_hi, dp_size // n_hi, ex_size), ("dy", "dz", "expert"))


def solution(mesh):
    inner = split_mesh(mesh)
    dp = ("dy", "dz")
    placed = (
        P("expert", dp, None),
        P("expert", dp, None),
        P("expert", dp, None),
        P("expert", dp, None),
        P("expert", dp, None),
        P(dp + ("expert",), None, None),
        P(dp + ("expert",), None),
        P(dp + ("expert",), None),
    )
    return jax.shard_map(
        body,
        mesh=inner,
        in_specs=placed,
        out_specs=(
            P("expert", dp, None),
            P("expert", dp, None),
            P("expert", dp, None),
            P(dp + ("expert",), None),
        ),
        check_vma=False,
    )
```

```python
import jax
import jax.numpy as jnp
import numpy as np
from jax import lax
from jax.sharding import Mesh
from jax.sharding import PartitionSpec as P

beta_one = 0.9
beta_two = 0.999
learn_rate = 0.002
tiny_eps = 1e-08
steps_done = 100.0


def adam_update(master, moment_one, moment_two, grad):
    m_new = beta_one * moment_one + (1.0 - beta_one) * grad
    v_new = beta_two * moment_two + (1.0 - beta_two) * grad * grad
    fix_one = 1.0 - beta_one**steps_done
    fix_two = 1.0 - beta_two**steps_done
    step_size = m_new / fix_one / (jnp.sqrt(v_new / fix_two) + tiny_eps)
    return (master - learn_rate * step_size, m_new, v_new)


def slot_places(routes, experts):
    flat = routes.reshape(-1)
    onehot = (flat[:, None] == jnp.arange(experts, dtype=jnp.int32)[None, :]).astype(jnp.int32)
    place = jnp.sum((jnp.cumsum(onehot, axis=0) - onehot) * onehot, axis=1)
    return (flat, place)


def body(master, moment_one, moment_two, saved_rows, saved_grads, slot_rows, routes, gates):
    n_hi = lax.axis_size("dy")
    n_lo = lax.axis_size("dz")
    experts = lax.axis_size("expert")

    rows_here = saved_rows[0]
    grads_here = saved_grads[0]
    saved, d_model = grads_here.shape
    group_width = d_model // n_hi
    rows_group = lax.all_gather(rows_here, "dy", axis=0, tiled=True)
    grads_group = lax.all_to_all(
        grads_here.reshape(saved, n_hi, group_width).transpose(1, 0, 2),
        "dy",
        split_axis=0,
        concat_axis=0,
        tiled=True,
    ).reshape(n_hi * saved, group_width)
    partial = lax.dot_general(
        grads_group, rows_group, (((0,), (0,)), ((), ())), preferred_element_type=jnp.float32
    ).astype(jnp.bfloat16)

    tok_count, top_count, width = slot_rows.shape
    capacity = tok_count * top_count * 5 // (4 * experts)
    flat, place = slot_places(routes, experts)
    slot_id = flat * capacity + place
    table = jnp.arange(experts * capacity, dtype=jnp.int32)
    select = (table[:, None] == slot_id[None, :]).astype(jnp.bfloat16)
    outgoing = lax.dot_general(
        select, slot_rows.reshape(-1, width), (((1,), (0,)), ((), ())),
        preferred_element_type=jnp.float32,
    ).astype(jnp.bfloat16).reshape(experts, capacity, width)
    received = lax.all_to_all(outgoing, "expert", split_axis=0, concat_axis=0, tiled=True)
    received, partial = lax.optimization_barrier((received, partial))
    shifted = [received]
    for step in range(1, n_hi):
        pairs = [(j, (j + step) % n_hi) for j in range(n_hi)]
        shifted.append(lax.ppermute(received, "dy", pairs))
    me_hi = lax.axis_index("dy")
    order = (me_hi - jnp.arange(n_hi, dtype=jnp.int32)) % n_hi
    slots_group = jnp.take(jnp.stack(shifted), order, axis=0).reshape(-1, width)

    grad = lax.psum_scatter(partial, "dz", scatter_dimension=0, tiled=True).astype(jnp.float32)
    master_new, m_new, v_new = adam_update(master[0], moment_one[0], moment_two[0], grad)
    weights_shard = master_new.astype(jnp.bfloat16)

    weights_group = lax.all_gather(weights_shard, "dz", axis=0, tiled=True)
    product = lax.dot_general(
        slots_group, weights_group, (((1,), (1,)), ((), ())), preferred_element_type=jnp.float32
    ).astype(jnp.bfloat16)
    returned = lax.all_to_all(
        product, ("dy", "expert"), split_axis=0, concat_axis=0, tiled=True
    ).reshape(n_hi, experts * capacity, group_width)

    slot_pairs = slot_id.reshape(tok_count, top_count)
    combine = jnp.sum(
        (slot_pairs[:, :, None] == table[None, None, :]).astype(jnp.float32) * gates[:, :, None],
        axis=1,
    )
    mixed = jnp.einsum(
        "ts,hsf->thf",
        combine,
        returned.astype(jnp.float32),
        precision=lax.Precision.HIGHEST,
        preferred_element_type=jnp.float32,
    )
    mixed = mixed.reshape(tok_count, n_hi * group_width).astype(jnp.bfloat16)
    return (master_new[None], m_new[None], v_new[None], mixed)


def split_mesh(mesh):
    devices = mesh.devices
    dp_size, ex_size = devices.shape
    column = devices[:, 0]
    try:
        n_hi = len({d.coords[1] for d in column})
    except Exception:
        n_hi = 1
    if n_hi < 1 or dp_size % n_hi:
        n_hi = 1
    return Mesh(devices.reshape(n_hi, dp_size // n_hi, ex_size), ("dy", "dz", "expert"))


def solution(mesh):
    inner = split_mesh(mesh)
    dp = ("dy", "dz")
    placed = (
        P("expert", dp, None),
        P("expert", dp, None),
        P("expert", dp, None),
        P("expert", dp, None),
        P("expert", dp, None),
        P(dp + ("expert",), None, None),
        P(dp + ("expert",), None),
        P(dp + ("expert",), None),
    )
    return jax.shard_map(
        body,
        mesh=inner,
        in_specs=placed,
        out_specs=(
            P("expert", dp, None),
            P("expert", dp, None),
            P("expert", dp, None),
            P(dp + ("expert",), None),
        ),
        check_vma=False,
    )
```

```python
import jax
import jax.numpy as jnp
import numpy as np
from jax import lax
from jax.sharding import Mesh
from jax.sharding import PartitionSpec as P

beta_one = 0.9
beta_two = 0.999
learn_rate = 0.002
tiny_eps = 1e-08
steps_done = 100.0


def adam_update(master, moment_one, moment_two, grad):
    m_new = beta_one * moment_one + (1.0 - beta_one) * grad
    v_new = beta_two * moment_two + (1.0 - beta_two) * grad * grad
    fix_one = 1.0 - beta_one**steps_done
    fix_two = 1.0 - beta_two**steps_done
    step_size = m_new / fix_one / (jnp.sqrt(v_new / fix_two) + tiny_eps)
    return (master - learn_rate * step_size, m_new, v_new)


def slot_places(routes, experts):
    flat = routes.reshape(-1)
    onehot = (flat[:, None] == jnp.arange(experts, dtype=jnp.int32)[None, :]).astype(jnp.int32)
    place = jnp.sum((jnp.cumsum(onehot, axis=0) - onehot) * onehot, axis=1)
    return (flat, place)


CHUNKS = 2


def body(master, moment_one, moment_two, saved_rows, saved_grads, slot_rows, routes, gates):
    n_hi = lax.axis_size("dy")
    n_lo = lax.axis_size("dz")
    experts = lax.axis_size("expert")
    chunks = CHUNKS

    rows_here = saved_rows[0]
    grads_here = saved_grads[0]
    saved, d_model = grads_here.shape
    group_width = d_model // n_hi
    own = group_width // n_lo
    piece = own // chunks
    rows_group = lax.all_gather(rows_here, "dy", axis=0, tiled=True)
    grads_sorted = grads_here.reshape(saved, n_hi, n_lo, chunks, piece).transpose(1, 3, 0, 2, 4)
    grads_group = lax.all_to_all(grads_sorted, "dy", split_axis=0, concat_axis=0, tiled=True)
    partials = []
    for h in range(chunks):
        cols = grads_group[:, h].reshape(n_hi * saved, n_lo * piece)
        partials.append(
            lax.dot_general(
                cols, rows_group, (((0,), (0,)), ((), ())), preferred_element_type=jnp.float32
            ).astype(jnp.bfloat16)
        )

    tok_count, top_count, width = slot_rows.shape
    capacity = tok_count * top_count * 5 // (4 * experts)
    flat, place = slot_places(routes, experts)
    slot_id = flat * capacity + place
    table = jnp.arange(experts * capacity, dtype=jnp.int32)
    select = (table[:, None] == slot_id[None, :]).astype(jnp.bfloat16)
    outgoing = lax.dot_general(
        select, slot_rows.reshape(-1, width), (((1,), (0,)), ((), ())),
        preferred_element_type=jnp.float32,
    ).astype(jnp.bfloat16).reshape(experts, capacity, width)
    received = lax.all_to_all(outgoing, "expert", split_axis=0, concat_axis=0, tiled=True)
    received, partials = lax.optimization_barrier((received, partials))
    me_hi = lax.axis_index("dy")
    slots_group = jnp.zeros((n_hi,) + received.shape, received.dtype)
    slots_group = lax.dynamic_update_slice(slots_group, received[None], (me_hi, 0, 0, 0))
    for step in range(1, n_hi):
        pairs = [(j, (j + step) % n_hi) for j in range(n_hi)]
        arrived = lax.ppermute(received, "dy", pairs)
        slots_group = lax.dynamic_update_slice(
            slots_group, arrived[None], ((me_hi - step) % n_hi, 0, 0, 0)
        )
    slots_group = slots_group.reshape(-1, width)

    slot_pairs = slot_id.reshape(tok_count, top_count)
    combine = jnp.sum(
        (slot_pairs[:, :, None] == table[None, None, :]).astype(jnp.float32) * gates[:, :, None],
        axis=1,
    )

    masters, firsts, seconds, mixes = [], [], [], []
    for h in range(chunks):
        grad = lax.psum_scatter(partials[h], "dz", scatter_dimension=0, tiled=True)
        rows = slice(h * piece, (h + 1) * piece)
        master_new, m_new, v_new = adam_update(
            master[0, rows], moment_one[0, rows], moment_two[0, rows], grad.astype(jnp.float32)
        )
        masters.append(master_new)
        firsts.append(m_new)
        seconds.append(v_new)
        weights_piece = lax.all_gather(master_new.astype(jnp.bfloat16), "dz", axis=0, tiled=True)
        product = lax.dot_general(
            slots_group, weights_piece, (((1,), (1,)), ((), ())),
            preferred_element_type=jnp.float32,
        ).astype(jnp.bfloat16)
        returned = lax.all_to_all(
            product, ("dy", "expert"), split_axis=0, concat_axis=0, tiled=True
        ).reshape(n_hi, experts * capacity, n_lo, piece)
        mixes.append(
            jnp.einsum(
                "ts,hszr->thzr",
                combine,
                returned.astype(jnp.float32),
                precision=lax.Precision.HIGHEST,
                preferred_element_type=jnp.float32,
            )
        )
    mixed = jnp.stack(mixes, axis=3).reshape(tok_count, d_model).astype(jnp.bfloat16)
    master_new = jnp.concatenate(masters, axis=0)
    m_new = jnp.concatenate(firsts, axis=0)
    v_new = jnp.concatenate(seconds, axis=0)
    return (master_new[None], m_new[None], v_new[None], mixed)


def split_mesh(mesh):
    devices = mesh.devices
    dp_size, ex_size = devices.shape
    column = devices[:, 0]
    try:
        n_hi = len({d.coords[1] for d in column})
    except Exception:
        n_hi = 1
    if n_hi < 1 or dp_size % n_hi:
        n_hi = 1
    return Mesh(devices.reshape(n_hi, dp_size // n_hi, ex_size), ("dy", "dz", "expert"))


def solution(mesh):
    inner = split_mesh(mesh)
    dp = ("dy", "dz")
    placed = (
        P("expert", dp, None),
        P("expert", dp, None),
        P("expert", dp, None),
        P("expert", dp, None),
        P("expert", dp, None),
        P(dp + ("expert",), None, None),
        P(dp + ("expert",), None),
        P(dp + ("expert",), None),
    )
    return jax.shard_map(
        body,
        mesh=inner,
        in_specs=placed,
        out_specs=(
            P("expert", dp, None),
            P("expert", dp, None),
            P("expert", dp, None),
            P(dp + ("expert",), None),
        ),
        check_vma=False,
    )
```

```python
import jax
import jax.numpy as jnp
import numpy as np
from jax import lax
from jax.sharding import Mesh
from jax.sharding import PartitionSpec as P

beta_one = 0.9
beta_two = 0.999
learn_rate = 0.002
tiny_eps = 1e-08
steps_done = 100.0


def adam_update(master, moment_one, moment_two, grad):
    m_new = beta_one * moment_one + (1.0 - beta_one) * grad
    v_new = beta_two * moment_two + (1.0 - beta_two) * grad * grad
    fix_one = 1.0 - beta_one**steps_done
    fix_two = 1.0 - beta_two**steps_done
    step_size = m_new / fix_one / (jnp.sqrt(v_new / fix_two) + tiny_eps)
    return (master - learn_rate * step_size, m_new, v_new)


def slot_places(routes, experts):
    flat = routes.reshape(-1)
    onehot = (flat[:, None] == jnp.arange(experts, dtype=jnp.int32)[None, :]).astype(jnp.int32)
    place = jnp.sum((jnp.cumsum(onehot, axis=0) - onehot) * onehot, axis=1)
    return (flat, place)


def body(master, moment_one, moment_two, saved_rows, saved_grads, slot_rows, routes, gates):
    ny_hi, ny_lo = lax.axis_size("yh"), lax.axis_size("yl")
    nz_hi, nz_lo = lax.axis_size("zh"), lax.axis_size("zl")
    experts = lax.axis_size("expert")
    near = ("yl", "zl")
    far = ("yh", "zh")
    n_near = ny_lo * nz_lo

    rows_here = saved_rows[0]
    grads_here = saved_grads[0]
    saved, d_model = grads_here.shape
    own = d_model // (ny_hi * ny_lo * nz_hi * nz_lo)
    rows_group = lax.all_gather(rows_here, near, axis=0, tiled=True)
    grads_sorted = grads_here.reshape(saved, ny_hi, ny_lo, nz_hi, nz_lo, own).transpose(
        2, 4, 0, 1, 3, 5
    ).reshape(n_near, saved, ny_hi * nz_hi * own)
    grads_group = lax.all_to_all(
        grads_sorted, near, split_axis=0, concat_axis=0, tiled=True
    ).reshape(n_near * saved, ny_hi * nz_hi * own)
    partial = lax.dot_general(
        grads_group, rows_group, (((0,), (0,)), ((), ())), preferred_element_type=jnp.float32
    ).astype(jnp.bfloat16)

    tok_count, top_count, width = slot_rows.shape
    capacity = tok_count * top_count * 5 // (4 * experts)
    flat, place = slot_places(routes, experts)
    slot_id = flat * capacity + place
    table = jnp.arange(experts * capacity, dtype=jnp.int32)
    select = (table[:, None] == slot_id[None, :]).astype(jnp.bfloat16)
    outgoing = lax.dot_general(
        select, slot_rows.reshape(-1, width), (((1,), (0,)), ((), ())),
        preferred_element_type=jnp.float32,
    ).astype(jnp.bfloat16).reshape(experts, capacity, width)
    received = lax.all_to_all(outgoing, "expert", split_axis=0, concat_axis=0, tiled=True)
    received, partial = lax.optimization_barrier((received, partial))
    me_near = lax.axis_index("yl") * nz_lo + lax.axis_index("zl")
    slots_group = jnp.zeros((n_near,) + received.shape, received.dtype)
    slots_group = lax.dynamic_update_slice(slots_group, received[None], (me_near, 0, 0, 0))
    for flip in range(1, n_near):
        pairs = [(j, j ^ flip) for j in range(n_near)]
        arrived = lax.ppermute(received, near, pairs)
        slots_group = lax.dynamic_update_slice(
            slots_group, arrived[None], (me_near ^ flip, 0, 0, 0)
        )
    slots_group = slots_group.reshape(-1, width)

    grad = lax.psum_scatter(partial, far, scatter_dimension=0, tiled=True).astype(jnp.float32)
    master_new, m_new, v_new = adam_update(master[0], moment_one[0], moment_two[0], grad)
    weights_shard = master_new.astype(jnp.bfloat16)

    weights_group = lax.all_gather(weights_shard, far, axis=0, tiled=True)
    product = lax.dot_general(
        slots_group, weights_group, (((1,), (1,)), ((), ())), preferred_element_type=jnp.float32
    ).astype(jnp.bfloat16)
    returned = lax.all_to_all(
        product, near + ("expert",), split_axis=0, concat_axis=0, tiled=True
    ).reshape(ny_lo, nz_lo, experts * capacity, ny_hi, nz_hi, own)

    slot_pairs = slot_id.reshape(tok_count, top_count)
    combine = jnp.sum(
        (slot_pairs[:, :, None] == table[None, None, :]).astype(jnp.float32) * gates[:, :, None],
        axis=1,
    )
    mixed = jnp.einsum(
        "ts,abshzr->thazbr",
        combine,
        returned.astype(jnp.float32),
        precision=lax.Precision.HIGHEST,
        preferred_element_type=jnp.float32,
    )
    mixed = mixed.reshape(tok_count, d_model).astype(jnp.bfloat16)
    return (master_new[None], m_new[None], v_new[None], mixed)


def split_mesh(mesh):
    devices = mesh.devices
    dp_size, ex_size = devices.shape
    column = devices[:, 0]
    try:
        n_y = len({d.coords[1] for d in column})
    except Exception:
        n_y = 1
    if n_y < 1 or dp_size % n_y:
        n_y = 1
    n_z = dp_size // n_y
    y_lo = 2 if n_y % 2 == 0 else 1
    z_lo = 2 if n_z % 2 == 0 else 1
    shape = (n_y // y_lo, y_lo, n_z // z_lo, z_lo, ex_size)
    return Mesh(devices.reshape(shape), ("yh", "yl", "zh", "zl", "expert"))


def solution(mesh):
    inner = split_mesh(mesh)
    dp = ("yh", "yl", "zh", "zl")
    placed = (
        P("expert", dp, None),
        P("expert", dp, None),
        P("expert", dp, None),
        P("expert", dp, None),
        P("expert", dp, None),
        P(dp + ("expert",), None, None),
        P(dp + ("expert",), None),
        P(dp + ("expert",), None),
    )
    return jax.shard_map(
        body,
        mesh=inner,
        in_specs=placed,
        out_specs=(
            P("expert", dp, None),
            P("expert", dp, None),
            P("expert", dp, None),
            P(dp + ("expert",), None),
        ),
        check_vma=False,
    )
```

```python
import jax
import jax.numpy as jnp
import numpy as np
from jax import lax
from jax.sharding import Mesh
from jax.sharding import PartitionSpec as P

beta_one = 0.9
beta_two = 0.999
learn_rate = 0.002
tiny_eps = 1e-08
steps_done = 100.0


def adam_update(master, moment_one, moment_two, grad):
    m_new = beta_one * moment_one + (1.0 - beta_one) * grad
    v_new = beta_two * moment_two + (1.0 - beta_two) * grad * grad
    fix_one = 1.0 - beta_one**steps_done
    fix_two = 1.0 - beta_two**steps_done
    step_size = m_new / fix_one / (jnp.sqrt(v_new / fix_two) + tiny_eps)
    return (master - learn_rate * step_size, m_new, v_new)


def slot_places(routes, experts):
    flat = routes.reshape(-1)
    onehot = (flat[:, None] == jnp.arange(experts, dtype=jnp.int32)[None, :]).astype(jnp.int32)
    place = jnp.sum((jnp.cumsum(onehot, axis=0) - onehot) * onehot, axis=1)
    return (flat, place)


def body(master, moment_one, moment_two, saved_rows, saved_grads, slot_rows, routes, gates):
    n_hi = lax.axis_size("dy")
    n_lo = lax.axis_size("dz")
    experts = lax.axis_size("expert")

    rows_here = saved_rows[0]
    grads_here = saved_grads[0]
    saved, d_model = grads_here.shape
    group_width = d_model // n_hi
    rows_group = lax.all_gather(rows_here, "dy", axis=0, tiled=True)
    grads_group = lax.all_to_all(
        grads_here.reshape(saved, n_hi, group_width).transpose(1, 0, 2),
        "dy",
        split_axis=0,
        concat_axis=0,
        tiled=True,
    ).reshape(n_hi * saved, group_width)
    partial = lax.dot_general(
        grads_group, rows_group, (((0,), (0,)), ((), ())), preferred_element_type=jnp.float32
    ).astype(jnp.bfloat16)

    tok_count, top_count, width = slot_rows.shape
    capacity = tok_count * top_count * 5 // (4 * experts)
    flat, place = slot_places(routes, experts)
    slot_id = flat * capacity + place
    table = jnp.arange(experts * capacity, dtype=jnp.int32)
    select = (table[:, None] == slot_id[None, :]).astype(jnp.bfloat16)
    outgoing = lax.dot_general(
        select, slot_rows.reshape(-1, width), (((1,), (0,)), ((), ())),
        preferred_element_type=jnp.float32,
    ).astype(jnp.bfloat16).reshape(experts, capacity, width)
    received = lax.all_to_all(outgoing, "expert", split_axis=0, concat_axis=0, tiled=True)
    received, partial = lax.optimization_barrier((received, partial))
    shifted = [received]
    for step in range(1, n_hi):
        pairs = [(j, (j + step) % n_hi) for j in range(n_hi)]
        shifted.append(lax.ppermute(received, "dy", pairs))
    me_hi = lax.axis_index("dy")

    grad = lax.psum_scatter(partial, "dz", scatter_dimension=0, tiled=True).astype(jnp.float32)
    master_new, m_new, v_new = adam_update(master[0], moment_one[0], moment_two[0], grad)
    weights_shard = master_new.astype(jnp.bfloat16)

    weights_group = lax.all_gather(weights_shard, "dz", axis=0, tiled=True)
    product = jnp.zeros((n_hi, experts * capacity, group_width), jnp.bfloat16)
    for step in range(n_hi):
        block = shifted[step].reshape(-1, width)
        part = lax.dot_general(
            block, weights_group, (((1,), (1,)), ((), ())), preferred_element_type=jnp.float32
        ).astype(jnp.bfloat16)
        product = lax.dynamic_update_slice(product, part[None], ((me_hi - step) % n_hi, 0, 0))
    product = product.reshape(-1, group_width)
    returned = lax.all_to_all(
        product, ("dy", "expert"), split_axis=0, concat_axis=0, tiled=True
    ).reshape(n_hi, experts * capacity, group_width)

    slot_pairs = slot_id.reshape(tok_count, top_count)
    combine = jnp.sum(
        (slot_pairs[:, :, None] == table[None, None, :]).astype(jnp.float32) * gates[:, :, None],
        axis=1,
    )
    mixed = jnp.einsum(
        "ts,hsf->thf",
        combine,
        returned.astype(jnp.float32),
        precision=lax.Precision.HIGHEST,
        preferred_element_type=jnp.float32,
    )
    mixed = mixed.reshape(tok_count, n_hi * group_width).astype(jnp.bfloat16)
    return (master_new[None], m_new[None], v_new[None], mixed)


def split_mesh(mesh):
    devices = mesh.devices
    dp_size, ex_size = devices.shape
    column = devices[:, 0]
    try:
        n_hi = len({d.coords[1] for d in column})
    except Exception:
        n_hi = 1
    if n_hi < 1 or dp_size % n_hi:
        n_hi = 1
    return Mesh(devices.reshape(n_hi, dp_size // n_hi, ex_size), ("dy", "dz", "expert"))


def solution(mesh):
    inner = split_mesh(mesh)
    dp = ("dy", "dz")
    placed = (
        P("expert", dp, None),
        P("expert", dp, None),
        P("expert", dp, None),
        P("expert", dp, None),
        P("expert", dp, None),
        P(dp + ("expert",), None, None),
        P(dp + ("expert",), None),
        P(dp + ("expert",), None),
    )
    return jax.shard_map(
        body,
        mesh=inner,
        in_specs=placed,
        out_specs=(
            P("expert", dp, None),
            P("expert", dp, None),
            P("expert", dp, None),
            P(dp + ("expert",), None),
        ),
        check_vma=False,
    )
```

```python
import jax
import jax.numpy as jnp
import numpy as np
from jax import lax
from jax.sharding import Mesh
from jax.sharding import PartitionSpec as P

beta_one = 0.9
beta_two = 0.999
learn_rate = 0.002
tiny_eps = 1e-08
steps_done = 100.0


def adam_update(master, moment_one, moment_two, grad):
    m_new = beta_one * moment_one + (1.0 - beta_one) * grad
    v_new = beta_two * moment_two + (1.0 - beta_two) * grad * grad
    fix_one = 1.0 - beta_one**steps_done
    fix_two = 1.0 - beta_two**steps_done
    step_size = m_new / fix_one / (jnp.sqrt(v_new / fix_two) + tiny_eps)
    return (master - learn_rate * step_size, m_new, v_new)


def slot_places(routes, experts):
    flat = routes.reshape(-1)
    onehot = (flat[:, None] == jnp.arange(experts, dtype=jnp.int32)[None, :]).astype(jnp.int32)
    place = jnp.sum((jnp.cumsum(onehot, axis=0) - onehot) * onehot, axis=1)
    return (flat, place)


def body(master, moment_one, moment_two, saved_rows, saved_grads, slot_rows, routes, gates):
    n_hi = lax.axis_size("dy")
    n_lo = lax.axis_size("dz")
    experts = lax.axis_size("expert")

    rows_here = saved_rows[0]
    grads_here = saved_grads[0]
    saved, d_model = grads_here.shape
    group_width = d_model // n_hi
    own = group_width // n_lo
    rows_group = lax.all_gather(rows_here, "dy", axis=0, tiled=True)
    grads_group = lax.all_to_all(
        grads_here.reshape(saved, n_hi, group_width).transpose(1, 0, 2),
        "dy",
        split_axis=0,
        concat_axis=0,
        tiled=True,
    ).reshape(n_hi * saved, group_width)
    partial = lax.dot_general(
        grads_group, rows_group, (((0,), (0,)), ((), ())), preferred_element_type=jnp.float32
    ).astype(jnp.bfloat16)

    tok_count, top_count, width = slot_rows.shape
    capacity = tok_count * top_count * 5 // (4 * experts)
    flat, place = slot_places(routes, experts)
    slot_id = flat * capacity + place
    table = jnp.arange(experts * capacity, dtype=jnp.int32)
    select = (table[:, None] == slot_id[None, :]).astype(jnp.bfloat16)
    outgoing = lax.dot_general(
        select, slot_rows.reshape(-1, width), (((1,), (0,)), ((), ())),
        preferred_element_type=jnp.float32,
    ).astype(jnp.bfloat16).reshape(experts, capacity, width)
    received = lax.all_to_all(outgoing, "expert", split_axis=0, concat_axis=0, tiled=True)
    received, partial = lax.optimization_barrier((received, partial))
    shifted = [received]
    for step in range(1, n_hi):
        pairs = [(j, (j + step) % n_hi) for j in range(n_hi)]
        shifted.append(lax.ppermute(received, "dy", pairs))
    me_hi = lax.axis_index("dy")

    grad = lax.psum_scatter(partial, "dz", scatter_dimension=0, tiled=True).astype(jnp.float32)
    master_new, m_new, v_new = adam_update(master[0], moment_one[0], moment_two[0], grad)
    weights_shard = master_new.astype(jnp.bfloat16)

    me_lo = lax.axis_index("dz")
    ahead = [(j, (j + 1) % n_lo) for j in range(n_lo)]
    behind = [(j, (j - 1) % n_lo) for j in range(n_lo)]
    blocks, owners = [weights_shard], [0]
    forward = backward = weights_shard
    for hop in range(1, n_lo // 2 + 1):
        forward = lax.ppermute(forward, "dz", ahead)
        blocks.append(forward)
        owners.append(-hop)
        if hop < n_lo - hop:
            backward = lax.ppermute(backward, "dz", behind)
            blocks.append(backward)
            owners.append(hop)
    split = min(len(blocks), 5)
    groups = [(0, split), (split, len(blocks))] if split < len(blocks) else [(0, split)]

    slot_pairs = slot_id.reshape(tok_count, top_count)
    combine = jnp.sum(
        (slot_pairs[:, :, None] == table[None, None, :]).astype(jnp.float32) * gates[:, :, None],
        axis=1,
    )
    pieces = []
    for first, last in groups:
        weights_group = jnp.concatenate(blocks[first:last], axis=0)
        count = last - first
        product = jnp.zeros((n_hi, experts * capacity, count * own), jnp.bfloat16)
        for step in range(n_hi):
            block = shifted[step].reshape(-1, width)
            part = lax.dot_general(
                block, weights_group, (((1,), (1,)), ((), ())), preferred_element_type=jnp.float32
            ).astype(jnp.bfloat16)
            product = lax.dynamic_update_slice(product, part[None], ((me_hi - step) % n_hi, 0, 0))
        returned = lax.all_to_all(
            product.reshape(-1, count * own), ("dy", "expert"), split_axis=0, concat_axis=0, tiled=True
        ).reshape(n_hi, experts * capacity, count, own)
        pieces.append(
            jnp.einsum(
                "ts,hsjr->thjr",
                combine,
                returned.astype(jnp.float32),
                precision=lax.Precision.HIGHEST,
                preferred_element_type=jnp.float32,
            )
        )
    gathered = jnp.concatenate(pieces, axis=2)
    where = (me_lo + jnp.asarray(owners, jnp.int32)) % n_lo
    placing = (where[:, None] == jnp.arange(n_lo, dtype=jnp.int32)[None, :]).astype(jnp.float32)
    mixed = jnp.einsum(
        "thjr,jb->thbr",
        gathered,
        placing,
        precision=lax.Precision.HIGHEST,
        preferred_element_type=jnp.float32,
    )
    mixed = mixed.reshape(tok_count, d_model).astype(jnp.bfloat16)
    return (master_new[None], m_new[None], v_new[None], mixed)


def split_mesh(mesh):
    devices = mesh.devices
    dp_size, ex_size = devices.shape
    column = devices[:, 0]
    try:
        n_hi = len({d.coords[1] for d in column})
    except Exception:
        n_hi = 1
    if n_hi < 1 or dp_size % n_hi:
        n_hi = 1
    return Mesh(devices.reshape(n_hi, dp_size // n_hi, ex_size), ("dy", "dz", "expert"))


def solution(mesh):
    inner = split_mesh(mesh)
    dp = ("dy", "dz")
    placed = (
        P("expert", dp, None),
        P("expert", dp, None),
        P("expert", dp, None),
        P("expert", dp, None),
        P("expert", dp, None),
        P(dp + ("expert",), None, None),
        P(dp + ("expert",), None),
        P(dp + ("expert",), None),
    )
    return jax.shard_map(
        body,
        mesh=inner,
        in_specs=placed,
        out_specs=(
            P("expert", dp, None),
            P("expert", dp, None),
            P("expert", dp, None),
            P(dp + ("expert",), None),
        ),
        check_vma=False,
    )
```

```python
import jax
import jax.numpy as jnp
import numpy as np
from jax import lax
from jax.sharding import Mesh
from jax.sharding import PartitionSpec as P

beta_one = 0.9
beta_two = 0.999
learn_rate = 0.002
tiny_eps = 1e-08
steps_done = 100.0


def adam_update(master, moment_one, moment_two, grad):
    m_new = beta_one * moment_one + (1.0 - beta_one) * grad
    v_new = beta_two * moment_two + (1.0 - beta_two) * grad * grad
    fix_one = 1.0 - beta_one**steps_done
    fix_two = 1.0 - beta_two**steps_done
    step_size = m_new / fix_one / (jnp.sqrt(v_new / fix_two) + tiny_eps)
    return (master - learn_rate * step_size, m_new, v_new)


def slot_places(routes, experts):
    flat = routes.reshape(-1)
    onehot = (flat[:, None] == jnp.arange(experts, dtype=jnp.int32)[None, :]).astype(jnp.int32)
    place = jnp.sum((jnp.cumsum(onehot, axis=0) - onehot) * onehot, axis=1)
    return (flat, place)


def body(master, moment_one, moment_two, saved_rows, saved_grads, slot_rows, routes, gates):
    n_hi = lax.axis_size("dy")
    n_lo = lax.axis_size("dz")
    experts = lax.axis_size("expert")

    rows_here = saved_rows[0]
    grads_here = saved_grads[0]
    saved, d_model = grads_here.shape
    group_width = d_model // n_hi
    rows_group = lax.all_gather(rows_here, "dy", axis=0, tiled=True)
    me_hi = lax.axis_index("dy")
    grads_split = grads_here.reshape(saved, n_hi, group_width)
    grads_group = jnp.zeros((n_hi, saved, group_width), grads_here.dtype)
    grads_group = lax.dynamic_update_slice(
        grads_group, lax.dynamic_index_in_dim(grads_split, me_hi, axis=1, keepdims=False)[None],
        (me_hi, 0, 0),
    )
    for step in range(1, n_hi):
        pairs = [(j, (j + step) % n_hi) for j in range(n_hi)]
        sent = lax.dynamic_index_in_dim(grads_split, (me_hi + step) % n_hi, axis=1, keepdims=False)
        arrived = lax.ppermute(sent, "dy", pairs)
        grads_group = lax.dynamic_update_slice(
            grads_group, arrived[None], ((me_hi - step) % n_hi, 0, 0)
        )
    grads_group = grads_group.reshape(n_hi * saved, group_width)
    partial = lax.dot_general(
        grads_group, rows_group, (((0,), (0,)), ((), ())), preferred_element_type=jnp.float32
    ).astype(jnp.bfloat16)

    tok_count, top_count, width = slot_rows.shape
    capacity = tok_count * top_count * 5 // (4 * experts)
    flat, place = slot_places(routes, experts)
    slot_id = flat * capacity + place
    table = jnp.arange(experts * capacity, dtype=jnp.int32)
    select = (table[:, None] == slot_id[None, :]).astype(jnp.bfloat16)
    outgoing = lax.dot_general(
        select, slot_rows.reshape(-1, width), (((1,), (0,)), ((), ())),
        preferred_element_type=jnp.float32,
    ).astype(jnp.bfloat16).reshape(experts, capacity, width)
    received = lax.all_to_all(outgoing, "expert", split_axis=0, concat_axis=0, tiled=True)
    received, partial = lax.optimization_barrier((received, partial))
    shifted = [received]
    for step in range(1, n_hi):
        pairs = [(j, (j + step) % n_hi) for j in range(n_hi)]
        shifted.append(lax.ppermute(received, "dy", pairs))

    grad = lax.psum_scatter(partial, "dz", scatter_dimension=0, tiled=True).astype(jnp.float32)
    master_new, m_new, v_new = adam_update(master[0], moment_one[0], moment_two[0], grad)
    weights_shard = master_new.astype(jnp.bfloat16)

    weights_group = lax.all_gather(weights_shard, "dz", axis=0, tiled=True)
    product = jnp.zeros((n_hi, experts * capacity, group_width), jnp.bfloat16)
    for step in range(n_hi):
        block = shifted[step].reshape(-1, width)
        part = lax.dot_general(
            block, weights_group, (((1,), (1,)), ((), ())), preferred_element_type=jnp.float32
        ).astype(jnp.bfloat16)
        product = lax.dynamic_update_slice(product, part[None], ((me_hi - step) % n_hi, 0, 0))
    product = product.reshape(-1, group_width)
    returned = lax.all_to_all(
        product, ("dy", "expert"), split_axis=0, concat_axis=0, tiled=True
    ).reshape(n_hi, experts * capacity, group_width)

    slot_pairs = slot_id.reshape(tok_count, top_count)
    combine = jnp.sum(
        (slot_pairs[:, :, None] == table[None, None, :]).astype(jnp.float32) * gates[:, :, None],
        axis=1,
    )
    mixed = jnp.einsum(
        "ts,hsf->thf",
        combine,
        returned.astype(jnp.float32),
        precision=lax.Precision.HIGHEST,
        preferred_element_type=jnp.float32,
    )
    mixed = mixed.reshape(tok_count, n_hi * group_width).astype(jnp.bfloat16)
    return (master_new[None], m_new[None], v_new[None], mixed)


def split_mesh(mesh):
    devices = mesh.devices
    dp_size, ex_size = devices.shape
    column = devices[:, 0]
    try:
        n_hi = len({d.coords[1] for d in column})
    except Exception:
        n_hi = 1
    if n_hi < 1 or dp_size % n_hi:
        n_hi = 1
    return Mesh(devices.reshape(n_hi, dp_size // n_hi, ex_size), ("dy", "dz", "expert"))


def solution(mesh):
    inner = split_mesh(mesh)
    dp = ("dy", "dz")
    placed = (
        P("expert", dp, None),
        P("expert", dp, None),
        P("expert", dp, None),
        P("expert", dp, None),
        P("expert", dp, None),
        P(dp + ("expert",), None, None),
        P(dp + ("expert",), None),
        P(dp + ("expert",), None),
    )
    return jax.shard_map(
        body,
        mesh=inner,
        in_specs=placed,
        out_specs=(
            P("expert", dp, None),
            P("expert", dp, None),
            P("expert", dp, None),
            P(dp + ("expert",), None),
        ),
        check_vma=False,
    )
```

```python
import jax
import jax.numpy as jnp
import numpy as np
from jax import lax
from jax.sharding import Mesh
from jax.sharding import PartitionSpec as P

beta_one = 0.9
beta_two = 0.999
learn_rate = 0.002
tiny_eps = 1e-08
steps_done = 100.0


def adam_update(master, moment_one, moment_two, grad):
    m_new = beta_one * moment_one + (1.0 - beta_one) * grad
    v_new = beta_two * moment_two + (1.0 - beta_two) * grad * grad
    fix_one = 1.0 - beta_one**steps_done
    fix_two = 1.0 - beta_two**steps_done
    step_size = m_new / fix_one / (jnp.sqrt(v_new / fix_two) + tiny_eps)
    return (master - learn_rate * step_size, m_new, v_new)


def slot_places(routes, experts):
    flat = routes.reshape(-1)
    onehot = (flat[:, None] == jnp.arange(experts, dtype=jnp.int32)[None, :]).astype(jnp.int32)
    place = jnp.sum((jnp.cumsum(onehot, axis=0) - onehot) * onehot, axis=1)
    return (flat, place)


def body(master, moment_one, moment_two, saved_rows, saved_grads, slot_rows, routes, gates):
    n_hi = lax.axis_size("dy")
    n_lo = lax.axis_size("dz")
    experts = lax.axis_size("expert")

    rows_here = saved_rows[0]
    grads_here = saved_grads[0]
    saved, d_model = grads_here.shape
    group_width = d_model // n_hi
    rows_group = lax.all_gather(rows_here, "dy", axis=0, tiled=True)
    grads_group = lax.all_to_all(
        grads_here.reshape(saved, n_hi, group_width).transpose(1, 0, 2),
        "dy",
        split_axis=0,
        concat_axis=0,
        tiled=True,
    ).reshape(n_hi * saved, group_width)
    partial = lax.dot_general(
        grads_group, rows_group, (((0,), (0,)), ((), ())), preferred_element_type=jnp.float32
    ).astype(jnp.bfloat16)

    tok_count, top_count, width = slot_rows.shape
    capacity = tok_count * top_count * 5 // (4 * experts)
    flat, place = slot_places(routes, experts)
    slot_id = flat * capacity + place
    table = jnp.arange(experts * capacity, dtype=jnp.int32)
    select = (table[:, None] == slot_id[None, :]).astype(jnp.bfloat16)
    outgoing = lax.dot_general(
        select, slot_rows.reshape(-1, width), (((1,), (0,)), ((), ())),
        preferred_element_type=jnp.float32,
    ).astype(jnp.bfloat16).reshape(experts, capacity, width)
    received = lax.all_to_all(outgoing, "expert", split_axis=0, concat_axis=0, tiled=True)
    received, partial = lax.optimization_barrier((received, partial))
    shifted = [received]
    for step in range(1, n_hi):
        pairs = [(j, (j + step) % n_hi) for j in range(n_hi)]
        shifted.append(lax.ppermute(received, "dy", pairs))
    me_hi = lax.axis_index("dy")

    grad = lax.psum_scatter(partial, "dz", scatter_dimension=0, tiled=True).astype(jnp.float32)
    weights_shard = adam_update(master[0], moment_one[0], moment_two[0], grad)[0].astype(jnp.bfloat16)
    state = lax.optimization_barrier((master[0], moment_one[0], moment_two[0], grad))
    master_new, m_new, v_new = adam_update(*state)

    weights_group = lax.all_gather(weights_shard, "dz", axis=0, tiled=True)
    product = jnp.zeros((n_hi, experts * capacity, group_width), jnp.bfloat16)
    for step in range(n_hi):
        block = shifted[step].reshape(-1, width)
        part = lax.dot_general(
            block, weights_group, (((1,), (1,)), ((), ())), preferred_element_type=jnp.float32
        ).astype(jnp.bfloat16)
        product = lax.dynamic_update_slice(product, part[None], ((me_hi - step) % n_hi, 0, 0))
    product = product.reshape(-1, group_width)
    returned = lax.all_to_all(
        product, ("dy", "expert"), split_axis=0, concat_axis=0, tiled=True
    ).reshape(n_hi, experts * capacity, group_width)

    slot_pairs = slot_id.reshape(tok_count, top_count)
    combine = jnp.sum(
        (slot_pairs[:, :, None] == table[None, None, :]).astype(jnp.float32) * gates[:, :, None],
        axis=1,
    )
    mixed = jnp.einsum(
        "ts,hsf->thf",
        combine,
        returned.astype(jnp.float32),
        precision=lax.Precision.HIGHEST,
        preferred_element_type=jnp.float32,
    )
    mixed = mixed.reshape(tok_count, n_hi * group_width).astype(jnp.bfloat16)
    return (master_new[None], m_new[None], v_new[None], mixed)


def split_mesh(mesh):
    devices = mesh.devices
    dp_size, ex_size = devices.shape
    column = devices[:, 0]
    try:
        n_hi = len({d.coords[1] for d in column})
    except Exception:
        n_hi = 1
    if n_hi < 1 or dp_size % n_hi:
        n_hi = 1
    return Mesh(devices.reshape(n_hi, dp_size // n_hi, ex_size), ("dy", "dz", "expert"))


def solution(mesh):
    inner = split_mesh(mesh)
    dp = ("dy", "dz")
    placed = (
        P("expert", dp, None),
        P("expert", dp, None),
        P("expert", dp, None),
        P("expert", dp, None),
        P("expert", dp, None),
        P(dp + ("expert",), None, None),
        P(dp + ("expert",), None),
        P(dp + ("expert",), None),
    )
    return jax.shard_map(
        body,
        mesh=inner,
        in_specs=placed,
        out_specs=(
            P("expert", dp, None),
            P("expert", dp, None),
            P("expert", dp, None),
            P(dp + ("expert",), None),
        ),
        check_vma=False,
    )
```

```python
import jax
import jax.numpy as jnp
import numpy as np
from jax import lax
from jax.sharding import Mesh
from jax.sharding import PartitionSpec as P

beta_one = 0.9
beta_two = 0.999
learn_rate = 0.002
tiny_eps = 1e-08
steps_done = 100.0


def adam_update(master, moment_one, moment_two, grad):
    m_new = beta_one * moment_one + (1.0 - beta_one) * grad
    v_new = beta_two * moment_two + (1.0 - beta_two) * grad * grad
    fix_one = 1.0 - beta_one**steps_done
    fix_two = 1.0 - beta_two**steps_done
    step_size = m_new / fix_one / (jnp.sqrt(v_new / fix_two) + tiny_eps)
    return (master - learn_rate * step_size, m_new, v_new)


def slot_places(routes, experts):
    flat = routes.reshape(-1)
    onehot = (flat[:, None] == jnp.arange(experts, dtype=jnp.int32)[None, :]).astype(jnp.int32)
    place = jnp.sum((jnp.cumsum(onehot, axis=0) - onehot) * onehot, axis=1)
    return (flat, place)


def body(master, moment_one, moment_two, saved_rows, saved_grads, slot_rows, routes, gates):
    n_hi = lax.axis_size("dy")
    n_lo = lax.axis_size("dz")
    experts = lax.axis_size("expert")

    rows_here = saved_rows[0]
    grads_here = saved_grads[0]
    saved, d_model = grads_here.shape
    group_width = d_model // n_hi
    rows_group = lax.all_gather(rows_here, "dy", axis=0, tiled=True)
    grads_group = lax.all_to_all(
        grads_here.reshape(saved, n_hi, group_width).transpose(1, 0, 2),
        "dy",
        split_axis=0,
        concat_axis=0,
        tiled=True,
    ).reshape(n_hi * saved, group_width)
    partial = lax.dot_general(
        grads_group, rows_group, (((0,), (0,)), ((), ())), preferred_element_type=jnp.float32
    ).astype(jnp.bfloat16)

    tok_count, top_count, width = slot_rows.shape
    capacity = tok_count * top_count * 5 // (4 * experts)
    flat, place = slot_places(routes, experts)
    slot_id = flat * capacity + place
    table = jnp.arange(experts * capacity, dtype=jnp.int32)
    select = (table[:, None] == slot_id[None, :]).astype(jnp.bfloat16)
    outgoing = lax.dot_general(
        select, slot_rows.reshape(-1, width), (((1,), (0,)), ((), ())),
        preferred_element_type=jnp.float32,
    ).astype(jnp.bfloat16).reshape(experts, capacity, width)
    received = lax.all_to_all(outgoing, "expert", split_axis=0, concat_axis=0, tiled=True)
    received, partial = lax.optimization_barrier((received, partial))
    shifted = [received]
    for step in range(1, n_hi):
        pairs = [(j, (j + step) % n_hi) for j in range(n_hi)]
        shifted.append(lax.ppermute(received, "dy", pairs))
    me_hi = lax.axis_index("dy")

    grad = lax.psum_scatter(partial, "dz", scatter_dimension=0, tiled=True).astype(jnp.float32)
    master_new, m_new, v_new = adam_update(master[0], moment_one[0], moment_two[0], grad)
    weights_shard = master_new.astype(jnp.bfloat16)

    weights_group = lax.all_gather(weights_shard, "dz", axis=0, tiled=True)
    product = jnp.zeros((n_hi, experts * capacity, group_width), jnp.bfloat16)
    for step in range(n_hi):
        block = shifted[step].reshape(-1, width)
        part = lax.dot_general(
            block, weights_group, (((1,), (1,)), ((), ())), preferred_element_type=jnp.float32
        ).astype(jnp.bfloat16)
        product = lax.dynamic_update_slice(product, part[None], ((me_hi - step) % n_hi, 0, 0))
    product = product.reshape(-1, group_width)
    returned = lax.all_to_all(
        product, ("dy", "expert"), split_axis=0, concat_axis=0, tiled=True
    ).reshape(n_hi, experts * capacity, group_width)

    slot_pairs = slot_id.reshape(tok_count, top_count)
    combine = jnp.sum(
        (slot_pairs[:, :, None] == table[None, None, :]).astype(jnp.float32) * gates[:, :, None],
        axis=1,
    )
    high = combine.astype(jnp.bfloat16)
    low = (combine - high.astype(jnp.float32)).astype(jnp.bfloat16)
    outputs = returned.transpose(1, 0, 2).reshape(experts * capacity, n_hi * group_width)
    mixed = sum(
        lax.dot_general(
            part, outputs, (((1,), (0,)), ((), ())), preferred_element_type=jnp.float32
        )
        for part in (high, low)
    ).astype(jnp.bfloat16)
    return (master_new[None], m_new[None], v_new[None], mixed)


def split_mesh(mesh):
    devices = mesh.devices
    dp_size, ex_size = devices.shape
    column = devices[:, 0]
    try:
        n_hi = len({d.coords[1] for d in column})
    except Exception:
        n_hi = 1
    if n_hi < 1 or dp_size % n_hi:
        n_hi = 1
    return Mesh(devices.reshape(n_hi, dp_size // n_hi, ex_size), ("dy", "dz", "expert"))


def solution(mesh):
    inner = split_mesh(mesh)
    dp = ("dy", "dz")
    placed = (
        P("expert", dp, None),
        P("expert", dp, None),
        P("expert", dp, None),
        P("expert", dp, None),
        P("expert", dp, None),
        P(dp + ("expert",), None, None),
        P(dp + ("expert",), None),
        P(dp + ("expert",), None),
    )
    return jax.shard_map(
        body,
        mesh=inner,
        in_specs=placed,
        out_specs=(
            P("expert", dp, None),
            P("expert", dp, None),
            P("expert", dp, None),
            P(dp + ("expert",), None),
        ),
        check_vma=False,
    )
```
